256 devices in a mesh: traj: 64 (over z, y, core), mstate: 4 (over x).
Axes of the slice: x: 4, y: 4, z: 8, core: 2. Of those that a mesh axis runs over, the one named last changes fastest.
Arguments:
- bias: float32 [32, 2097152], P(None, ('traj', 'mstate')), may hold values from -206 to 206
- labels: int32 [2097152], P(('traj', 'mstate')), may hold values from 0 to 4095, as said below
- therm_index: int32 [2097152], P(('traj', 'mstate')), may hold values from 0 to 31
- counts: int32 [32, 4096, 4096], P(None, 'traj', 'mstate'), may hold values from 0 to 4, as said below
- free_start: float32 [32, 4096], replicated, may hold values from -6 to 6
- mult_start: float32 [32, 4096], replicated, may hold values from -6 to 6
Outputs:
- free_energy: float32 [32, 4096], P(None, 'mstate')
- log_mult: float32 [32, 4096], P(None, 'mstate')
The draws below stay inside these ranges and needn't reach their ends.
Inputs may be any that keep to these rules, and one draw needn't show every extreme that they name: `labels`: every Markov state is the label of at least one frame. `counts`: most entries are zero.
All inputs are finite; a program needn't handle non-finite values.
Results may differ from the reference program's by a relative error of at most 0.0001.
Values sent between devices are 32-bit elements; how exact they have to be, the bound alone decides.
No kernel may reach another device: no remote copies, remote signals or barrier semaphores. Data moves between devices by JAX's collectives and lax.ppermute only.
A program may use at most 64 MiB of HBM per device.

```python
import jax
import jax.numpy as jnp
from jax import lax

K = 32
M = 4096
ITERS = 2
FRAMES = 2097152


def forced_frames(key):
    return jax.random.permutation(jax.random.fold_in(key, 7), FRAMES)[:M]


def draw_labels(key, part):
    first_key, second_key = jax.random.split(jax.random.fold_in(key, 11), 2)
    first = jax.random.randint(first_key, (FRAMES,), 0, M)
    second = jax.random.randint(second_key, (FRAMES,), 0, M)
    base = jnp.minimum(first, second).astype(jnp.int32)
    chosen = forced_frames(key)
    filled = base.at[chosen].set(jnp.arange(M, dtype=jnp.int32))
    return filled.astype(jnp.int32)


def draw_bias(key, part):
    first_key = jax.random.fold_in(jax.random.fold_in(key, 23), 0)
    values = jnp.clip(2.0 * jax.random.normal(first_key, (K, FRAMES), jnp.float32), -12.0, 12.0)
    return values.astype(jnp.float32)


def draw_counts(key, part):
    place_key, entry_key = jax.random.split(jax.random.fold_in(key, 37))
    place = jax.random.randint(place_key, (K, M, M), 0, M).astype(jnp.int32)
    packed = jax.random.randint(entry_key, (K, M, M), 0, 16777216).astype(jnp.int32)
    present = place < 2
    exponent = jnp.right_shift(packed, 16) % 3
    mantissa = jnp.bitwise_and(jnp.right_shift(packed, 8), 255)
    low_bits = jnp.left_shift(jnp.ones_like(exponent), exponent) - 1
    entry_value = 1 + jnp.bitwise_and(mantissa, low_bits)
    return jnp.where(present, entry_value, 0).astype(jnp.int32)


def set_ends(values, key, smallest, top_value):
    index_at = [jax.random.randint(jax.random.fold_in(key, axis), (), 0, length) for axis, length in enumerate(values.shape)]
    widest = values.shape.index(max(values.shape))
    neighbour = index_at[:widest] + [(index_at[widest] + 1) % values.shape[widest]] + index_at[widest + 1:]
    return values.at[tuple(index_at)].set(smallest).at[tuple(neighbour)].set(top_value)


def normal_values(own_key, extent, width, bound, kind=jnp.bfloat16):
    result = width * jax.random.normal(own_key, extent, jnp.float32)
    return jnp.clip(result, min=-bound, max=bound).astype(kind)


def setup_inputs(seed: int = 0) -> dict:
    splits = jax.random.split(jax.random.key(seed), 7)
    return {
        "bias": draw_bias(jax.random.fold_in(splits[6], 71), 0),
        "labels": draw_labels(jax.random.fold_in(splits[6], 71), 0),
        "therm_index": set_ends(jax.random.randint(splits[2], (FRAMES,), 0, K), jax.random.fold_in(splits[2], 1), 0, K - 1).astype(jnp.int32),
        "counts": draw_counts(jax.random.fold_in(splits[6], 71), 0),
        "free_start": normal_values(splits[4], (K, M), 1.0, 6.0, jnp.float32),
        "mult_start": normal_values(splits[5], (K, M), 1.0, 6.0, jnp.float32),
    }


def update_mult(counts, free, mult):
    def per_state(args):
        block, fk, vk = args
        weight = jax.nn.sigmoid(vk[None, :] + fk[:, None] - vk[:, None] - fk[None, :])
        return jnp.sum(block.astype(fk.dtype) * weight, axis=0)

    total = lax.map(per_state, (counts, free, mult))
    return jnp.log(0.5 + total)


def reference(bias, labels, therm_index, counts, free_start, mult_start):
    ftype = bias.dtype
    states = jax.nn.one_hot(therm_index, K, dtype=ftype)
    visits = jax.ops.segment_sum(states, labels, num_segments=M).T
    free, mult = free_start, mult_start
    for step in range(ITERS):
        mult = update_mult(counts, free, mult)
        level = jnp.log(jnp.exp(mult) + visits) + free
        scores = jnp.take(level, labels, axis=1) - bias
        top = jnp.max(scores, axis=0)
        logl = top + jnp.log(jnp.sum(jnp.exp(scores - top[None, :]), axis=0))
        term = -bias - logl[None, :]
        shift = jnp.max(term, axis=1)
        weights = jnp.exp(term - shift[:, None])
        total = jax.ops.segment_sum(weights.T, labels, num_segments=M).T
        free = -(shift[:, None] + jnp.log(total))
    return free, mult
```

```python
import jax
import jax.numpy as jnp
from jax import lax
from jax.sharding import PartitionSpec as P

ITERS = 2


def _xor_pairs(n, bit):
    return [(i, i ^ bit) for i in range(n)]


def _bits(n):
    bit = 1
    while bit < n:
        yield bit
        bit *= 2


def _tree_sum(x, axis, n):
    for bit in _bits(n):
        x = x + lax.ppermute(x, axis, _xor_pairs(n, bit))
    return x


def _lse_merge(top, total, other_top, other_total):
    both = jnp.maximum(top, other_top)
    scaled = total * jnp.exp(top - both)[:, None] + other_total * jnp.exp(other_top - both)[:, None]
    return both, scaled


def _lse_tree(top, total, axis, n):
    for bit in _bits(n):
        other_top, other_total = lax.ppermute((top, total), axis, _xor_pairs(n, bit))
        top, total = _lse_merge(top, total, other_top, other_total)
    return top, total


def _halve(x, axis, n, combine):
    index = lax.axis_index(axis)
    width = x.shape[1]
    bit = n // 2
    while bit >= 1:
        width //= 2
        side = (index // bit) % 2
        keep = lax.dynamic_slice_in_dim(x, side * width, width, 1)
        send = lax.dynamic_slice_in_dim(x, (1 - side) * width, width, 1)
        x = combine(keep, send, bit)
        bit //= 2
    return x


def _sum_halve(x, axis, n):
    return _halve(x, axis, n, lambda keep, send, bit: keep + lax.ppermute(send, axis, _xor_pairs(n, bit)))


def _lse_halve(top, total, axis, n):
    state = {"top": top}

    def combine(keep, send, bit):
        other_top, other = lax.ppermute((state["top"], send), axis, _xor_pairs(n, bit))
        state["top"], merged = _lse_merge(state["top"], keep, other_top, other)
        return merged

    rows = _halve(total, axis, n, combine)
    return state["top"], rows


def _frame_part(level, bias, labels, width):
    scores = jnp.take(level, labels, axis=1) - bias
    top = jnp.max(scores, axis=0)
    logl = top + jnp.log(jnp.sum(jnp.exp(scores - top[None, :]), axis=0))
    term = -bias - logl[None, :]
    local_top = jnp.max(term, axis=1)
    weights = jnp.exp(term - local_top[:, None])
    local_total = jax.ops.segment_sum(weights.T, labels, num_segments=width).T
    return local_top, local_total


def _mult_part(counts_real, free_cols, mult_cols, free_rows, mult_rows):
    weight = jax.nn.sigmoid(
        mult_rows[:, None, :]
        + free_cols[:, :, None]
        - mult_cols[:, :, None]
        - free_rows[:, None, :]
    )
    return jnp.sum(counts_real * weight, axis=1)


def per_device(bias, labels, therm_index, counts, free_start, mult_start):
    n_traj = lax.psum(1, "traj")
    n_mstate = lax.psum(1, "mstate")
    states_k = bias.shape[0]
    width = free_start.shape[1]
    col_count = counts.shape[1]
    row_count = counts.shape[2]
    traj_at = lax.axis_index("traj")
    mstate_at = lax.axis_index("mstate")
    col_start = traj_at * col_count
    row_start = mstate_at * row_count
    per_row = row_count // col_count

    col_pairs = []
    for src_t in range(n_traj):
        for c in range(n_mstate):
            dst_t = c * per_row + src_t // n_mstate
            dst_m = src_t % n_mstate
            col_pairs.append((src_t * n_mstate + c, dst_t * n_mstate + dst_m))
    col_offset = (traj_at // n_mstate) * col_count

    states = jax.nn.one_hot(therm_index, states_k, dtype=jnp.float32)
    local_visits = jax.ops.segment_sum(states, labels, num_segments=width).T
    visits_part = _sum_halve(local_visits, "mstate", n_mstate)
    counts_real = counts.astype(jnp.float32)

    free_cols = lax.dynamic_slice_in_dim(free_start, col_start, col_count, 1)
    mult_cols = lax.dynamic_slice_in_dim(mult_start, col_start, col_count, 1)
    free_rows = lax.dynamic_slice_in_dim(free_start, row_start, row_count, 1)
    mult_rows = lax.dynamic_slice_in_dim(mult_start, row_start, row_count, 1)
    visits_rows = None
    for step in range(ITERS):
        partial_rows = _mult_part(counts_real, free_cols, mult_cols, free_rows, mult_rows)
        if step == 0:
            both = _tree_sum(jnp.concatenate([partial_rows, visits_part], axis=1), "traj", n_traj)
            row_total, visits_rows = both[:, :row_count], both[:, row_count:]
        else:
            row_total = _tree_sum(partial_rows, "traj", n_traj)
        mult_rows = jnp.log(0.5 + row_total)
        level_rows = jnp.log(jnp.exp(mult_rows) + visits_rows) + free_rows
        level = lax.all_gather(level_rows, "mstate", axis=1, tiled=True)
        local_top, local_total = _frame_part(level, bias, labels, width)
        top, total = _lse_halve(local_top, local_total, "mstate", n_mstate)
        top, total = _lse_tree(top, total, "traj", n_traj)
        free_rows = -(top[:, None] + jnp.log(total))
        if step + 1 < ITERS:
            block = jnp.stack([
                lax.dynamic_slice_in_dim(free_rows, col_offset, col_count, 1),
                lax.dynamic_slice_in_dim(mult_rows, col_offset, col_count, 1),
            ])
            block = lax.ppermute(block, ("traj", "mstate"), col_pairs)
            free_cols, mult_cols = block[0], block[1]
    return (free_rows, mult_rows)


def solution(mesh):
    placed = (
        P(None, ("traj", "mstate")),
        P(("traj", "mstate")),
        P(("traj", "mstate")),
        P(None, "traj", "mstate"),
        P(),
        P(),
    )
    return jax.shard_map(
        per_device,
        mesh=mesh,
        in_specs=placed,
        out_specs=(P(None, "mstate"), P(None, "mstate")),
        check_vma=False,
    )
```

```python
import jax
import jax.numpy as jnp
from jax import lax
from jax.sharding import PartitionSpec as P

ITERS = 2


def _xor_pairs(n, bit):
    return [(i, i ^ bit) for i in range(n)]


def _add(a, b):
    return a + b


def _lse_merge(a, b):
    top = jnp.maximum(a[:, -1:], b[:, -1:])
    body = a[:, :-1] * jnp.exp(a[:, -1:] - top) + b[:, :-1] * jnp.exp(b[:, -1:] - top)
    return jnp.concatenate([body, top], axis=1)


def _tree(x, axis, n, merge):
    shift = 1
    while shift < n:
        wide = 4 if shift * 4 <= n else 2
        got = [lax.ppermute(x, axis, _xor_pairs(n, j * shift)) for j in range(1, wide)]
        if wide == 4:
            x = merge(merge(x, got[0]), merge(got[1], got[2]))
        else:
            x = merge(x, got[0])
        shift *= wide
    return x


def _scatter_blocks(x, axis, n, merge, extra=None):
    index = lax.axis_index(axis)
    width = x.shape[1] // n

    def block(b):
        piece = lax.dynamic_slice_in_dim(x, b * width, width, 1)
        return piece if extra is None else jnp.concatenate([piece, extra], axis=1)

    own = block(index)
    got = [lax.ppermute(block(index ^ j), axis, _xor_pairs(n, j)) for j in range(1, n)]
    while got:
        own = merge(own, got.pop(0))
    return own


def _gather_blocks(x, axis, n):
    index = lax.axis_index(axis)
    width = x.shape[1]
    full = jnp.zeros((x.shape[0], width * n), x.dtype)
    full = lax.dynamic_update_slice_in_dim(full, x, index * width, 1)
    for j in range(1, n):
        got = lax.ppermute(x, axis, _xor_pairs(n, j))
        full = lax.dynamic_update_slice_in_dim(full, got, (index ^ j) * width, 1)
    return full


def _frame_part(level, bias, labels, width):
    scores = jnp.take(level, labels, axis=1) - bias
    top = jnp.max(scores, axis=0)
    logl = top + jnp.log(jnp.sum(jnp.exp(scores - top[None, :]), axis=0))
    term = -bias - logl[None, :]
    local_top = jnp.max(term, axis=1)
    weights = jnp.exp(term - local_top[:, None])
    local_total = jax.ops.segment_sum(weights.T, labels, num_segments=width).T
    return local_top, local_total


def _mult_part(counts_real, free_cols, mult_cols, free_rows, mult_rows):
    weight = jax.nn.sigmoid(
        mult_rows[:, None, :]
        + free_cols[:, :, None]
        - mult_cols[:, :, None]
        - free_rows[:, None, :]
    )
    return jnp.sum(counts_real * weight, axis=1)


def per_device(bias, labels, therm_index, counts, free_start, mult_start):
    n_traj = lax.psum(1, "traj")
    n_mstate = lax.psum(1, "mstate")
    states_k = bias.shape[0]
    width = free_start.shape[1]
    col_count = counts.shape[1]
    row_count = counts.shape[2]
    traj_at = lax.axis_index("traj")
    mstate_at = lax.axis_index("mstate")
    col_start = traj_at * col_count
    row_start = mstate_at * row_count
    per_row = row_count // col_count

    col_pairs = []
    for src_t in range(n_traj):
        for c in range(n_mstate):
            dst_t = c * per_row + src_t // n_mstate
            dst_m = src_t % n_mstate
            col_pairs.append((src_t * n_mstate + c, dst_t * n_mstate + dst_m))
    col_offset = (traj_at // n_mstate) * col_count

    states = jax.nn.one_hot(therm_index, states_k, dtype=jnp.float32)
    local_visits = jax.ops.segment_sum(states, labels, num_segments=width).T
    visits_part = _scatter_blocks(local_visits, "mstate", n_mstate, _add)
    counts_real = counts.astype(jnp.float32)

    free_cols = lax.dynamic_slice_in_dim(free_start, col_start, col_count, 1)
    mult_cols = lax.dynamic_slice_in_dim(mult_start, col_start, col_count, 1)
    free_rows = lax.dynamic_slice_in_dim(free_start, row_start, row_count, 1)
    mult_rows = lax.dynamic_slice_in_dim(mult_start, row_start, row_count, 1)
    visits_rows = None
    for step in range(ITERS):
        partial_rows = _mult_part(counts_real, free_cols, mult_cols, free_rows, mult_rows)
        if step == 0:
            both = _tree(jnp.concatenate([partial_rows, visits_part], axis=1), "traj", n_traj, _add)
            row_total, visits_rows = both[:, :row_count], both[:, row_count:]
        else:
            row_total = _tree(partial_rows, "traj", n_traj, _add)
        mult_rows = jnp.log(0.5 + row_total)
        level_rows = jnp.log(jnp.exp(mult_rows) + visits_rows) + free_rows
        level = _gather_blocks(level_rows, "mstate", n_mstate)
        local_top, local_total = _frame_part(level, bias, labels, width)
        packed = _scatter_blocks(local_total, "mstate", n_mstate, _lse_merge, local_top[:, None])
        packed = _tree(packed, "traj", n_traj, _lse_merge)
        free_rows = -(packed[:, -1:] + jnp.log(packed[:, :-1]))
        if step + 1 < ITERS:
            block = jnp.stack([
                lax.dynamic_slice_in_dim(free_rows, col_offset, col_count, 1),
                lax.dynamic_slice_in_dim(mult_rows, col_offset, col_count, 1),
            ])
            block = lax.ppermute(block, ("traj", "mstate"), col_pairs)
            free_cols, mult_cols = block[0], block[1]
    return (free_rows, mult_rows)


def solution(mesh):
    placed = (
        P(None, ("traj", "mstate")),
        P(("traj", "mstate")),
        P(("traj", "mstate")),
        P(None, "traj", "mstate"),
        P(),
        P(),
    )
    return jax.shard_map(
        per_device,
        mesh=mesh,
        in_specs=placed,
        out_specs=(P(None, "mstate"), P(None, "mstate")),
        check_vma=False,
    )
```

```python
import jax
import jax.numpy as jnp
from jax import lax
from jax.experimental import pallas as pl
from jax.experimental.pallas import tpu as pltpu
from jax.sharding import PartitionSpec as P

ITERS = 2


def _xor_pairs(n, bit):
    return [(i, i ^ bit) for i in range(n)]


def _add(a, b):
    return a + b


def _lse_merge(a, b):
    top = jnp.maximum(a[:, -1:], b[:, -1:])
    body = a[:, :-1] * jnp.exp(a[:, -1:] - top) + b[:, :-1] * jnp.exp(b[:, -1:] - top)
    return jnp.concatenate([body, top], axis=1)


def _tree(x, axis, n, merge):
    shift = 1
    while shift < n:
        wide = 4 if shift * 4 <= n else 2
        got = [lax.ppermute(x, axis, _xor_pairs(n, j * shift)) for j in range(1, wide)]
        if wide == 4:
            x = merge(merge(x, got[0]), merge(got[1], got[2]))
        else:
            x = merge(x, got[0])
        shift *= wide
    return x


def _scatter_blocks(x, axis, n, merge, extra=None):
    index = lax.axis_index(axis)
    width = x.shape[1] // n

    def block(b):
        piece = lax.dynamic_slice_in_dim(x, b * width, width, 1)
        return piece if extra is None else jnp.concatenate([piece, extra], axis=1)

    own = block(index)
    got = [lax.ppermute(block(index ^ j), axis, _xor_pairs(n, j)) for j in range(1, n)]
    while got:
        own = merge(own, got.pop(0))
    return own


def _gather_blocks(x, axis, n):
    index = lax.axis_index(axis)
    width = x.shape[1]
    full = jnp.zeros((x.shape[0], width * n), x.dtype)
    full = lax.dynamic_update_slice_in_dim(full, x, index * width, 1)
    for j in range(1, n):
        got = lax.ppermute(x, axis, _xor_pairs(n, j))
        full = lax.dynamic_update_slice_in_dim(full, got, (index ^ j) * width, 1)
    return full


def _scatter_kernel(lab_ref, w_ref, o_ref, *accs):
    unroll = len(accs)
    for acc in accs:
        acc[...] = jnp.zeros_like(acc)

    def body(c, carry):
        base = c * unroll
        for j in range(unroll):
            x = base + j
            i = lab_ref[x]
            accs[j][pl.ds(i, 1), :] += w_ref[pl.ds(x, 1), :]
        return carry

    lax.fori_loop(0, w_ref.shape[0] // unroll, body, 0)
    total = accs[0][...]
    for acc in accs[1:]:
        total = total + acc[...]
    o_ref[...] = total


def _seg_rows(w_t, labels, width, unroll=8):
    return pl.pallas_call(
        _scatter_kernel,
        in_specs=[pl.BlockSpec(memory_space=pltpu.SMEM), pl.BlockSpec(memory_space=pltpu.VMEM)],
        out_specs=pl.BlockSpec(memory_space=pltpu.VMEM),
        out_shape=jax.ShapeDtypeStruct((width, w_t.shape[1]), jnp.float32),
        scratch_shapes=[pltpu.VMEM((width, w_t.shape[1]), jnp.float32)] * unroll,
    )(labels, w_t)


def _gather_kernel(lab_ref, lev_ref, o_ref):
    unroll = 16

    def body(c, carry):
        base = c * unroll
        for j in range(unroll):
            x = base + j
            o_ref[pl.ds(x, 1), :] = lev_ref[pl.ds(lab_ref[x], 1), :]
        return carry

    lax.fori_loop(0, o_ref.shape[0] // unroll, body, 0)


def _take_rows(lev_t, labels):
    return pl.pallas_call(
        _gather_kernel,
        in_specs=[pl.BlockSpec(memory_space=pltpu.SMEM), pl.BlockSpec(memory_space=pltpu.VMEM)],
        out_specs=pl.BlockSpec(memory_space=pltpu.VMEM),
        out_shape=jax.ShapeDtypeStruct((labels.shape[0], lev_t.shape[1]), lev_t.dtype),
    )(labels, lev_t)


def _frame_part(level, bias_t, labels, width):
    scores = _take_rows(level.T, labels) - bias_t
    top = jnp.max(scores, axis=1)
    logl = top + jnp.log(jnp.sum(jnp.exp(scores - top[:, None]), axis=1))
    term = -bias_t - logl[:, None]
    local_top = jnp.max(term, axis=0)
    weights = jnp.exp(term - local_top[None, :])
    local_total = _seg_rows(weights, labels, width).T
    return local_top, local_total


def _mult_part(counts_real, free_cols, mult_cols, free_rows, mult_rows):
    weight = jax.nn.sigmoid(
        mult_rows[:, None, :]
        + free_cols[:, :, None]
        - mult_cols[:, :, None]
        - free_rows[:, None, :]
    )
    return jnp.sum(counts_real * weight, axis=1)


def per_device(bias, labels, therm_index, counts, free_start, mult_start):
    n_traj = lax.psum(1, "traj")
    n_mstate = lax.psum(1, "mstate")
    states_k = bias.shape[0]
    width = free_start.shape[1]
    col_count = counts.shape[1]
    row_count = counts.shape[2]
    traj_at = lax.axis_index("traj")
    mstate_at = lax.axis_index("mstate")
    col_start = traj_at * col_count
    row_start = mstate_at * row_count
    per_row = row_count // col_count

    col_pairs = []
    for src_t in range(n_traj):
        for c in range(n_mstate):
            dst_t = c * per_row + src_t // n_mstate
            dst_m = src_t % n_mstate
            col_pairs.append((src_t * n_mstate + c, dst_t * n_mstate + dst_m))
    col_offset = (traj_at // n_mstate) * col_count

    states = jax.nn.one_hot(therm_index, states_k, dtype=jnp.float32)
    local_visits = _seg_rows(states, labels, width).T
    bias_t = bias.T
    visits_part = _scatter_blocks(local_visits, "mstate", n_mstate, _add)
    counts_real = counts.astype(jnp.float32)

    free_cols = lax.dynamic_slice_in_dim(free_start, col_start, col_count, 1)
    mult_cols = lax.dynamic_slice_in_dim(mult_start, col_start, col_count, 1)
    free_rows = lax.dynamic_slice_in_dim(free_start, row_start, row_count, 1)
    mult_rows = lax.dynamic_slice_in_dim(mult_start, row_start, row_count, 1)
    visits_rows = None
    for step in range(ITERS):
        partial_rows = _mult_part(counts_real, free_cols, mult_cols, free_rows, mult_rows)
        if step == 0:
            both = _tree(jnp.concatenate([partial_rows, visits_part], axis=1), "traj", n_traj, _add)
            row_total, visits_rows = both[:, :row_count], both[:, row_count:]
        else:
            row_total = _tree(partial_rows, "traj", n_traj, _add)
        mult_rows = jnp.log(0.5 + row_total)
        level_rows = jnp.log(jnp.exp(mult_rows) + visits_rows) + free_rows
        level = _gather_blocks(level_rows, "mstate", n_mstate)
        local_top, local_total = _frame_part(level, bias_t, labels, width)
        packed = _scatter_blocks(local_total, "mstate", n_mstate, _lse_merge, local_top[:, None])
        packed = _tree(packed, "traj", n_traj, _lse_merge)
        free_rows = -(packed[:, -1:] + jnp.log(packed[:, :-1]))
        if step + 1 < ITERS:
            block = jnp.stack([
                lax.dynamic_slice_in_dim(free_rows, col_offset, col_count, 1),
                lax.dynamic_slice_in_dim(mult_rows, col_offset, col_count, 1),
            ])
            block = lax.ppermute(block, ("traj", "mstate"), col_pairs)
            free_cols, mult_cols = block[0], block[1]
    return (free_rows, mult_rows)


def solution(mesh):
    placed = (
        P(None, ("traj", "mstate")),
        P(("traj", "mstate")),
        P(("traj", "mstate")),
        P(None, "traj", "mstate"),
        P(),
        P(),
    )
    return jax.shard_map(
        per_device,
        mesh=mesh,
        in_specs=placed,
        out_specs=(P(None, "mstate"), P(None, "mstate")),
        check_vma=False,
    )
```

```python
import jax
import jax.numpy as jnp
from jax import lax
from jax.experimental import pallas as pl
from jax.experimental.pallas import tpu as pltpu
from jax.sharding import PartitionSpec as P

ITERS = 2


def _xor_pairs(n, bit):
    return [(i, i ^ bit) for i in range(n)]


def _send(x, axis, pairs):
    return lax.ppermute(x.reshape(-1), axis, pairs).reshape(x.shape)


def _add(a, b):
    return a + b


def _lse_merge(a, b):
    top = jnp.maximum(a[:, -1:], b[:, -1:])
    body = a[:, :-1] * jnp.exp(a[:, -1:] - top) + b[:, :-1] * jnp.exp(b[:, -1:] - top)
    return jnp.concatenate([body, top], axis=1)


def _tree(x, axis, n, merge):
    shift = 1
    while shift < n:
        wide = 4 if shift * 4 <= n else 2
        got = [_send(x, axis, _xor_pairs(n, j * shift)) for j in range(1, wide)]
        if wide == 4:
            x = merge(merge(x, got[0]), merge(got[1], got[2]))
        else:
            x = merge(x, got[0])
        shift *= wide
    return x


def _scatter_blocks(x, axis, n, merge, extra=None):
    index = lax.axis_index(axis)
    width = x.shape[1] // n

    def block(b):
        piece = lax.dynamic_slice_in_dim(x, b * width, width, 1)
        return piece if extra is None else jnp.concatenate([piece, extra], axis=1)

    own = block(index)
    got = [_send(block(index ^ j), axis, _xor_pairs(n, j)) for j in range(1, n)]
    while got:
        own = merge(own, got.pop(0))
    return own


def _gather_blocks(x, axis, n):
    index = lax.axis_index(axis)
    width = x.shape[1]
    full = jnp.zeros((x.shape[0], width * n), x.dtype)
    full = lax.dynamic_update_slice_in_dim(full, x, index * width, 1)
    for j in range(1, n):
        got = _send(x, axis, _xor_pairs(n, j))
        full = lax.dynamic_update_slice_in_dim(full, got, (index ^ j) * width, 1)
    return full


def _scatter_kernel(lab_ref, w_ref, o_ref, *accs):
    unroll = len(accs)
    for acc in accs:
        acc[...] = jnp.zeros_like(acc)

    def body(c, carry):
        base = c * unroll
        for j in range(unroll):
            x = base + j
            i = lab_ref[x]
            accs[j][pl.ds(i, 1), :] += w_ref[pl.ds(x, 1), :]
        return carry

    lax.fori_loop(0, w_ref.shape[0] // unroll, body, 0)
    total = accs[0][...]
    for acc in accs[1:]:
        total = total + acc[...]
    o_ref[...] = total


def _seg_rows(w_t, labels, width, unroll=8):
    return pl.pallas_call(
        _scatter_kernel,
        in_specs=[pl.BlockSpec(memory_space=pltpu.SMEM), pl.BlockSpec(memory_space=pltpu.VMEM)],
        out_specs=pl.BlockSpec(memory_space=pltpu.VMEM),
        out_shape=jax.ShapeDtypeStruct((width, w_t.shape[1]), jnp.float32),
        scratch_shapes=[pltpu.VMEM((width, w_t.shape[1]), jnp.float32)] * unroll,
    )(labels, w_t)


def _gather_kernel(lab_ref, lev_ref, o_ref):
    unroll = 16

    def body(c, carry):
        base = c * unroll
        for j in range(unroll):
            x = base + j
            o_ref[pl.ds(x, 1), :] = lev_ref[pl.ds(lab_ref[x], 1), :]
        return carry

    lax.fori_loop(0, o_ref.shape[0] // unroll, body, 0)


def _take_rows(lev_t, labels):
    return pl.pallas_call(
        _gather_kernel,
        in_specs=[pl.BlockSpec(memory_space=pltpu.SMEM), pl.BlockSpec(memory_space=pltpu.VMEM)],
        out_specs=pl.BlockSpec(memory_space=pltpu.VMEM),
        out_shape=jax.ShapeDtypeStruct((labels.shape[0], lev_t.shape[1]), lev_t.dtype),
    )(labels, lev_t)


def _frame_part(level, bias_t, labels, width):
    scores = _take_rows(level.T, labels) - bias_t
    top = jnp.max(scores, axis=1)
    logl = top + jnp.log(jnp.sum(jnp.exp(scores - top[:, None]), axis=1))
    term = -bias_t - logl[:, None]
    local_top = jnp.max(term, axis=0)
    weights = jnp.exp(term - local_top[None, :])
    local_total = _seg_rows(weights, labels, width).T
    return local_top, local_total


def _mult_part(counts_real, free_cols, mult_cols, free_rows, mult_rows):
    weight = jax.nn.sigmoid(
        mult_rows[:, None, :]
        + free_cols[:, :, None]
        - mult_cols[:, :, None]
        - free_rows[:, None, :]
    )
    return jnp.sum(counts_real * weight, axis=1)


def per_device(bias, labels, therm_index, counts, free_start, mult_start):
    n_traj = lax.psum(1, "traj")
    n_mstate = lax.psum(1, "mstate")
    states_k = bias.shape[0]
    width = free_start.shape[1]
    col_count = counts.shape[1]
    row_count = counts.shape[2]
    traj_at = lax.axis_index("traj")
    mstate_at = lax.axis_index("mstate")
    col_start = traj_at * col_count
    row_start = mstate_at * row_count
    per_row = row_count // col_count

    col_pairs = []
    for src_t in range(n_traj):
        for c in range(n_mstate):
            dst_t = c * per_row + src_t // n_mstate
            dst_m = src_t % n_mstate
            col_pairs.append((src_t * n_mstate + c, dst_t * n_mstate + dst_m))
    col_offset = (traj_at // n_mstate) * col_count

    states = jax.nn.one_hot(therm_index, states_k, dtype=jnp.float32)
    local_visits = _seg_rows(states, labels, width).T
    bias_t = bias.T
    visits_part = _scatter_blocks(local_visits, "mstate", n_mstate, _add)
    counts_real = counts.astype(jnp.float32)

    free_cols = lax.dynamic_slice_in_dim(free_start, col_start, col_count, 1)
    mult_cols = lax.dynamic_slice_in_dim(mult_start, col_start, col_count, 1)
    free_rows = lax.dynamic_slice_in_dim(free_start, row_start, row_count, 1)
    mult_rows = lax.dynamic_slice_in_dim(mult_start, row_start, row_count, 1)
    visits_rows = None
    for step in range(ITERS):
        partial_rows = _mult_part(counts_real, free_cols, mult_cols, free_rows, mult_rows)
        if step == 0:
            both = _tree(jnp.concatenate([partial_rows, visits_part], axis=1), "traj", n_traj, _add)
            row_total, visits_rows = both[:, :row_count], both[:, row_count:]
        else:
            row_total = _tree(partial_rows, "traj", n_traj, _add)
        mult_rows = jnp.log(0.5 + row_total)
        level_rows = jnp.log(jnp.exp(mult_rows) + visits_rows) + free_rows
        level = _gather_blocks(level_rows, "mstate", n_mstate)
        local_top, local_total = _frame_part(level, bias_t, labels, width)
        packed = _scatter_blocks(local_total, "mstate", n_mstate, _lse_merge, local_top[:, None])
        packed = _tree(packed, "traj", n_traj, _lse_merge)
        free_rows = -(packed[:, -1:] + jnp.log(packed[:, :-1]))
        if step + 1 < ITERS:
            block = jnp.stack([
                lax.dynamic_slice_in_dim(free_rows, col_offset, col_count, 1),
                lax.dynamic_slice_in_dim(mult_rows, col_offset, col_count, 1),
            ])
            block = _send(block, ("traj", "mstate"), col_pairs)
            free_cols, mult_cols = block[0], block[1]
    return (free_rows, mult_rows)


def solution(mesh):
    placed = (
        P(None, ("traj", "mstate")),
        P(("traj", "mstate")),
        P(("traj", "mstate")),
        P(None, "traj", "mstate"),
        P(),
        P(),
    )
    return jax.shard_map(
        per_device,
        mesh=mesh,
        in_specs=placed,
        out_specs=(P(None, "mstate"), P(None, "mstate")),
        check_vma=False,
    )
```

```python
import jax
import jax.numpy as jnp
from jax import lax
from jax.experimental import pallas as pl
from jax.experimental.pallas import tpu as pltpu
from jax.sharding import PartitionSpec as P

ITERS = 2


def _xor_pairs(n, bit):
    return [(i, i ^ bit) for i in range(n)]


def _send(x, axis, pairs):
    return lax.ppermute(x.reshape(-1), axis, pairs).reshape(x.shape)


def _add(a, b):
    return a + b


def _lse_merge(a, b):
    top = jnp.maximum(a[:, -1:], b[:, -1:])
    body = a[:, :-1] * jnp.exp(a[:, -1:] - top) + b[:, :-1] * jnp.exp(b[:, -1:] - top)
    return jnp.concatenate([body, top], axis=1)


def _tree(x, axis, n, merge, most=8):
    shift = 1
    while shift < n:
        wide = 2
        while wide < most and shift * wide * 2 <= n:
            wide *= 2
        vals = [x] + [_send(x, axis, _xor_pairs(n, j * shift)) for j in range(1, wide)]
        while len(vals) > 1:
            vals = [merge(vals[i], vals[i + 1]) for i in range(0, len(vals), 2)]
        x = vals[0]
        shift *= wide
    return x


def _scatter_blocks(x, axis, n, merge, extra=None):
    index = lax.axis_index(axis)
    width = x.shape[1] // n

    def block(b):
        piece = lax.dynamic_slice_in_dim(x, b * width, width, 1)
        return piece if extra is None else jnp.concatenate([piece, extra], axis=1)

    own = block(index)
    got = [_send(block(index ^ j), axis, _xor_pairs(n, j)) for j in range(1, n)]
    while got:
        own = merge(own, got.pop(0))
    return own


def _gather_blocks(x, axis, n):
    index = lax.axis_index(axis)
    width = x.shape[1]
    full = jnp.zeros((x.shape[0], width * n), x.dtype)
    full = lax.dynamic_update_slice_in_dim(full, x, index * width, 1)
    for j in range(1, n):
        got = _send(x, axis, _xor_pairs(n, j))
        full = lax.dynamic_update_slice_in_dim(full, got, (index ^ j) * width, 1)
    return full


def _scatter_kernel(lab_ref, w_ref, o_ref, *accs):
    unroll = len(accs)
    for acc in accs:
        acc[...] = jnp.zeros_like(acc)

    def body(c, carry):
        base = c * unroll
        for j in range(unroll):
            x = base + j
            i = lab_ref[x]
            accs[j][pl.ds(i, 1), :] += w_ref[pl.ds(x, 1), :]
        return carry

    lax.fori_loop(0, w_ref.shape[0] // unroll, body, 0)
    total = accs[0][...]
    for acc in accs[1:]:
        total = total + acc[...]
    o_ref[...] = total


def _seg_rows(w_t, labels, width, unroll=8):
    return pl.pallas_call(
        _scatter_kernel,
        in_specs=[pl.BlockSpec(memory_space=pltpu.SMEM), pl.BlockSpec(memory_space=pltpu.VMEM)],
        out_specs=pl.BlockSpec(memory_space=pltpu.VMEM),
        out_shape=jax.ShapeDtypeStruct((width, w_t.shape[1]), jnp.float32),
        scratch_shapes=[pltpu.VMEM((width, w_t.shape[1]), jnp.float32)] * unroll,
    )(labels, w_t)


def _gather_kernel(lab_ref, lev_ref, o_ref):
    unroll = 16

    def body(c, carry):
        base = c * unroll
        for j in range(unroll):
            x = base + j
            o_ref[pl.ds(x, 1), :] = lev_ref[pl.ds(lab_ref[x], 1), :]
        return carry

    lax.fori_loop(0, o_ref.shape[0] // unroll, body, 0)


def _take_rows(lev_t, labels):
    return pl.pallas_call(
        _gather_kernel,
        in_specs=[pl.BlockSpec(memory_space=pltpu.SMEM), pl.BlockSpec(memory_space=pltpu.VMEM)],
        out_specs=pl.BlockSpec(memory_space=pltpu.VMEM),
        out_shape=jax.ShapeDtypeStruct((labels.shape[0], lev_t.shape[1]), lev_t.dtype),
    )(labels, lev_t)


def _frame_part(level, bias_t, labels, width):
    scores = _take_rows(level.T, labels) - bias_t
    top = jnp.max(scores, axis=1)
    logl = top + jnp.log(jnp.sum(jnp.exp(scores - top[:, None]), axis=1))
    term = -bias_t - logl[:, None]
    local_top = jnp.max(term, axis=0)
    weights = jnp.exp(term - local_top[None, :])
    local_total = _seg_rows(weights, labels, width).T
    return local_top, local_total


def _mult_part(counts_real, free_cols, mult_cols, free_rows, mult_rows):
    weight = jax.nn.sigmoid(
        mult_rows[:, None, :]
        + free_cols[:, :, None]
        - mult_cols[:, :, None]
        - free_rows[:, None, :]
    )
    return jnp.sum(counts_real * weight, axis=1)


def per_device(bias, labels, therm_index, counts, free_start, mult_start):
    n_traj = lax.psum(1, "traj")
    n_mstate = lax.psum(1, "mstate")
    states_k = bias.shape[0]
    width = free_start.shape[1]
    col_count = counts.shape[1]
    row_count = counts.shape[2]
    traj_at = lax.axis_index("traj")
    mstate_at = lax.axis_index("mstate")
    col_start = traj_at * col_count
    row_start = mstate_at * row_count
    per_row = row_count // col_count

    col_pairs = []
    for src_t in range(n_traj):
        for c in range(n_mstate):
            dst_t = c * per_row + src_t // n_mstate
            dst_m = src_t % n_mstate
            col_pairs.append((src_t * n_mstate + c, dst_t * n_mstate + dst_m))
    col_offset = (traj_at // n_mstate) * col_count

    states = jax.nn.one_hot(therm_index, states_k, dtype=jnp.float32)
    local_visits = _seg_rows(states, labels, width).T
    bias_t = bias.T
    visits_part = _scatter_blocks(local_visits, "mstate", n_mstate, _add)
    counts_real = counts.astype(jnp.float32)

    free_cols = lax.dynamic_slice_in_dim(free_start, col_start, col_count, 1)
    mult_cols = lax.dynamic_slice_in_dim(mult_start, col_start, col_count, 1)
    free_rows = lax.dynamic_slice_in_dim(free_start, row_start, row_count, 1)
    mult_rows = lax.dynamic_slice_in_dim(mult_start, row_start, row_count, 1)
    visits_rows = None
    for step in range(ITERS):
        partial_rows = _mult_part(counts_real, free_cols, mult_cols, free_rows, mult_rows)
        if step == 0:
            both = _tree(jnp.concatenate([partial_rows, visits_part], axis=1), "traj", n_traj, _add)
            row_total, visits_rows = both[:, :row_count], both[:, row_count:]
        else:
            row_total = _tree(partial_rows, "traj", n_traj, _add)
        mult_rows = jnp.log(0.5 + row_total)
        level_rows = jnp.log(jnp.exp(mult_rows) + visits_rows) + free_rows
        level = _gather_blocks(level_rows, "mstate", n_mstate)
        local_top, local_total = _frame_part(level, bias_t, labels, width)
        packed = _scatter_blocks(local_total, "mstate", n_mstate, _lse_merge, local_top[:, None])
        packed = _tree(packed, "traj", n_traj, _lse_merge)
        free_rows = -(packed[:, -1:] + jnp.log(packed[:, :-1]))
        if step + 1 < ITERS:
            block = jnp.stack([
                lax.dynamic_slice_in_dim(free_rows, col_offset, col_count, 1),
                lax.dynamic_slice_in_dim(mult_rows, col_offset, col_count, 1),
            ])
            block = _send(block, ("traj", "mstate"), col_pairs)
            free_cols, mult_cols = block[0], block[1]
    return (free_rows, mult_rows)


def solution(mesh):
    placed = (
        P(None, ("traj", "mstate")),
        P(("traj", "mstate")),
        P(("traj", "mstate")),
        P(None, "traj", "mstate"),
        P(),
        P(),
    )
    return jax.shard_map(
        per_device,
        mesh=mesh,
        in_specs=placed,
        out_specs=(P(None, "mstate"), P(None, "mstate")),
        check_vma=False,
    )
```

```python
import jax
import jax.numpy as jnp
from jax import lax
from jax.experimental import pallas as pl
from jax.experimental.pallas import tpu as pltpu
from jax.sharding import PartitionSpec as P

ITERS = 2


def _xor_pairs(n, bit):
    return [(i, i ^ bit) for i in range(n)]


def _send(x, axis, pairs):
    return lax.ppermute(x.reshape(-1), axis, pairs).reshape(x.shape)


def _add(a, b):
    return a + b


def _lse_merge(a, b):
    top = jnp.maximum(a[:, -1:], b[:, -1:])
    body = a[:, :-1] * jnp.exp(a[:, -1:] - top) + b[:, :-1] * jnp.exp(b[:, -1:] - top)
    return jnp.concatenate([body, top], axis=1)


def _tree(x, axis, n, merge):
    shift = 1
    while shift < n:
        wide = 4 if shift * 4 <= n else 2
        got = [_send(x, axis, _xor_pairs(n, j * shift)) for j in range(1, wide)]
        if wide == 4:
            x = merge(merge(x, got[0]), merge(got[1], got[2]))
        else:
            x = merge(x, got[0])
        shift *= wide
    return x


def _scatter_blocks(x, axis, n, merge, extra=None):
    index = lax.axis_index(axis)
    width = x.shape[1] // n

    def block(b):
        piece = lax.dynamic_slice_in_dim(x, b * width, width, 1)
        return piece if extra is None else jnp.concatenate([piece, extra], axis=1)

    own = block(index)
    got = [_send(block(index ^ j), axis, _xor_pairs(n, j)) for j in range(1, n)]
    while got:
        own = merge(own, got.pop(0))
    return own


def _gather_blocks(x, axis, n):
    index = lax.axis_index(axis)
    width = x.shape[1]
    full = jnp.zeros((x.shape[0], width * n), x.dtype)
    full = lax.dynamic_update_slice_in_dim(full, x, index * width, 1)
    for j in range(1, n):
        got = _send(x, axis, _xor_pairs(n, j))
        full = lax.dynamic_update_slice_in_dim(full, got, (index ^ j) * width, 1)
    return full


def _scatter_kernel(lab_ref, w_ref, o_ref, *accs):
    unroll = len(accs)
    for acc in accs:
        acc[...] = jnp.zeros_like(acc)

    def body(c, carry):
        base = c * unroll
        for j in range(unroll):
            x = base + j
            i = lab_ref[x]
            accs[j][pl.ds(i, 1), :] += w_ref[pl.ds(x, 1), :]
        return carry

    lax.fori_loop(0, w_ref.shape[0] // unroll, body, 0)
    total = accs[0][...]
    for acc in accs[1:]:
        total = total + acc[...]
    o_ref[...] = total


def _seg_rows(w_t, labels, width, unroll=8):
    return pl.pallas_call(
        _scatter_kernel,
        in_specs=[pl.BlockSpec(memory_space=pltpu.SMEM), pl.BlockSpec(memory_space=pltpu.VMEM)],
        out_specs=pl.BlockSpec(memory_space=pltpu.VMEM),
        out_shape=jax.ShapeDtypeStruct((width, w_t.shape[1]), jnp.float32),
        scratch_shapes=[pltpu.VMEM((width, w_t.shape[1]), jnp.float32)] * unroll,
    )(labels, w_t)


def _gather_kernel(lab_ref, lev_ref, o_ref):
    unroll = 16

    def body(c, carry):
        base = c * unroll
        for j in range(unroll):
            x = base + j
            o_ref[pl.ds(x, 1), :] = lev_ref[pl.ds(lab_ref[x], 1), :]
        return carry

    lax.fori_loop(0, o_ref.shape[0] // unroll, body, 0)


def _take_rows(lev_t, labels):
    return pl.pallas_call(
        _gather_kernel,
        in_specs=[pl.BlockSpec(memory_space=pltpu.SMEM), pl.BlockSpec(memory_space=pltpu.VMEM)],
        out_specs=pl.BlockSpec(memory_space=pltpu.VMEM),
        out_shape=jax.ShapeDtypeStruct((labels.shape[0], lev_t.shape[1]), lev_t.dtype),
    )(labels, lev_t)


def _frame_part(level, bias_t, labels, width):
    scores = _take_rows(level.T, labels) - bias_t
    top = jnp.max(scores, axis=1)
    logl = top + jnp.log(jnp.sum(jnp.exp(scores - top[:, None]), axis=1))
    term = -bias_t - logl[:, None]
    local_top = jnp.max(term, axis=0)
    weights = jnp.exp(term - local_top[None, :])
    local_total = _seg_rows(weights, labels, width).T
    return local_top, local_total


def _mult_part(counts_real, free_cols, mult_cols, free_rows, mult_rows):
    weight = jax.nn.sigmoid(
        mult_rows[:, None, :]
        + free_cols[:, :, None]
        - mult_cols[:, :, None]
        - free_rows[:, None, :]
    )
    return jnp.sum(counts_real * weight, axis=1)


def per_device(bias, labels, therm_index, counts, free_start, mult_start):
    n_traj = lax.psum(1, "traj")
    n_mstate = lax.psum(1, "mstate")
    states_k = bias.shape[0]
    width = free_start.shape[1]
    col_count = counts.shape[1]
    row_count = counts.shape[2]
    traj_at = lax.axis_index("traj")
    mstate_at = lax.axis_index("mstate")
    col_start = traj_at * col_count
    row_start = mstate_at * row_count
    per_row = row_count // col_count

    col_pairs = []
    for src_t in range(n_traj):
        for c in range(n_mstate):
            dst_t = c * per_row + src_t // n_mstate
            dst_m = src_t % n_mstate
            col_pairs.append((src_t * n_mstate + c, dst_t * n_mstate + dst_m))
    col_offset = (traj_at // n_mstate) * col_count

    states = jax.nn.one_hot(therm_index, states_k, dtype=jnp.float32)
    local_visits = _seg_rows(states, labels, width).T
    bias_t = bias.T
    visits_part = _scatter_blocks(local_visits, "mstate", n_mstate, _add)
    counts_real = counts.astype(jnp.float32)

    free_cols = lax.dynamic_slice_in_dim(free_start, col_start, col_count, 1)
    mult_cols = lax.dynamic_slice_in_dim(mult_start, col_start, col_count, 1)
    free_rows = lax.dynamic_slice_in_dim(free_start, row_start, row_count, 1)
    mult_rows = lax.dynamic_slice_in_dim(mult_start, row_start, row_count, 1)
    visits_rows = None
    for step in range(ITERS):
        partial_rows = _mult_part(counts_real, free_cols, mult_cols, free_rows, mult_rows)
        row_total = _tree(partial_rows, "traj", n_traj, _add)
        if step == 0:
            visits_rows = _tree(visits_part, "traj", n_traj, _add)
        mult_rows = jnp.log(0.5 + row_total)
        level_rows = jnp.log(jnp.exp(mult_rows) + visits_rows) + free_rows
        level = _gather_blocks(level_rows, "mstate", n_mstate)
        local_top, local_total = _frame_part(level, bias_t, labels, width)
        packed = _scatter_blocks(local_total, "mstate", n_mstate, _lse_merge, local_top[:, None])
        packed = _tree(packed, "traj", n_traj, _lse_merge)
        free_rows = -(packed[:, -1:] + jnp.log(packed[:, :-1]))
        if step + 1 < ITERS:
            block = jnp.stack([
                lax.dynamic_slice_in_dim(free_rows, col_offset, col_count, 1),
                lax.dynamic_slice_in_dim(mult_rows, col_offset, col_count, 1),
            ])
            block = _send(block, ("traj", "mstate"), col_pairs)
            free_cols, mult_cols = block[0], block[1]
    return (free_rows, mult_rows)


def solution(mesh):
    placed = (
        P(None, ("traj", "mstate")),
        P(("traj", "mstate")),
        P(("traj", "mstate")),
        P(None, "traj", "mstate"),
        P(),
        P(),
    )
    return jax.shard_map(
        per_device,
        mesh=mesh,
        in_specs=placed,
        out_specs=(P(None, "mstate"), P(None, "mstate")),
        check_vma=False,
    )
```

```python
import jax
import jax.numpy as jnp
from jax import lax
from jax.experimental import pallas as pl
from jax.experimental.pallas import tpu as pltpu
from jax.sharding import PartitionSpec as P

ITERS = 2


def _xor_pairs(n, bit):
    return [(i, i ^ bit) for i in range(n)]


def _send(x, axis, pairs):
    return lax.ppermute(x.reshape(-1), axis, pairs).reshape(x.shape)


def _add(a, b):
    return a + b


def _lse_merge(a, b):
    top = jnp.maximum(a[:, -1:], b[:, -1:])
    body = a[:, :-1] * jnp.exp(a[:, -1:] - top) + b[:, :-1] * jnp.exp(b[:, -1:] - top)
    return jnp.concatenate([body, top], axis=1)


def _tree(x, axis, n, merge):
    shift = 1
    while shift < n:
        wide = 4 if shift * 4 <= n else 2
        got = [_send(x, axis, _xor_pairs(n, j * shift)) for j in range(1, wide)]
        if wide == 4:
            x = merge(merge(x, got[0]), merge(got[1], got[2]))
        else:
            x = merge(x, got[0])
        shift *= wide
    return x


def _scatter_blocks(x, axis, n, merge, extra=None):
    index = lax.axis_index(axis)
    width = x.shape[1] // n

    def block(b):
        piece = lax.dynamic_slice_in_dim(x, b * width, width, 1)
        return piece if extra is None else jnp.concatenate([piece, extra], axis=1)

    own = block(index)
    got = [_send(block(index ^ j), axis, _xor_pairs(n, j)) for j in range(1, n)]
    while got:
        own = merge(own, got.pop(0))
    return own


def _gather_blocks(x, axis, n):
    index = lax.axis_index(axis)
    width = x.shape[1]
    full = jnp.zeros((x.shape[0], width * n), x.dtype)
    full = lax.dynamic_update_slice_in_dim(full, x, index * width, 1)
    for j in range(1, n):
        got = _send(x, axis, _xor_pairs(n, j))
        full = lax.dynamic_update_slice_in_dim(full, got, (index ^ j) * width, 1)
    return full


def _scatter_kernel(lab_ref, w_ref, o_ref, *accs):
    unroll = len(accs)
    for acc in accs:
        acc[...] = jnp.zeros_like(acc)

    def body(c, carry):
        base = c * unroll
        for j in range(unroll):
            x = base + j
            i = lab_ref[x]
            accs[j][pl.ds(i, 1), :] += w_ref[pl.ds(x, 1), :]
        return carry

    lax.fori_loop(0, w_ref.shape[0] // unroll, body, 0)
    total = accs[0][...]
    for acc in accs[1:]:
        total = total + acc[...]
    o_ref[...] = total


def _seg_rows(w_t, labels, width, unroll=8):
    return pl.pallas_call(
        _scatter_kernel,
        in_specs=[pl.BlockSpec(memory_space=pltpu.SMEM), pl.BlockSpec(memory_space=pltpu.VMEM)],
        out_specs=pl.BlockSpec(memory_space=pltpu.VMEM),
        out_shape=jax.ShapeDtypeStruct((width, w_t.shape[1]), jnp.float32),
        scratch_shapes=[pltpu.VMEM((width, w_t.shape[1]), jnp.float32)] * unroll,
    )(labels, w_t)


def _gather_kernel(lab_ref, lev_ref, o_ref):
    unroll = 16

    def body(c, carry):
        base = c * unroll
        for j in range(unroll):
            x = base + j
            o_ref[pl.ds(x, 1), :] = lev_ref[pl.ds(lab_ref[x], 1), :]
        return carry

    lax.fori_loop(0, o_ref.shape[0] // unroll, body, 0)


def _take_rows(lev_t, labels):
    return pl.pallas_call(
        _gather_kernel,
        in_specs=[pl.BlockSpec(memory_space=pltpu.SMEM), pl.BlockSpec(memory_space=pltpu.VMEM)],
        out_specs=pl.BlockSpec(memory_space=pltpu.VMEM),
        out_shape=jax.ShapeDtypeStruct((labels.shape[0], lev_t.shape[1]), lev_t.dtype),
    )(labels, lev_t)


def _frame_part(level_t, bias_t, labels, width):
    scores = _take_rows(level_t, labels) - bias_t
    top = jnp.max(scores, axis=1)
    logl = top + jnp.log(jnp.sum(jnp.exp(scores - top[:, None]), axis=1))
    term = -bias_t - logl[:, None]
    local_top = jnp.max(term, axis=0)
    weights = jnp.exp(term - local_top[None, :])
    local_total = _seg_rows(weights, labels, width).T
    return local_top, local_total


def _mult_part(counts_real, free_cols, mult_cols, free_rows, mult_rows):
    weight = jax.nn.sigmoid(
        mult_rows[:, None, :]
        + free_cols[:, :, None]
        - mult_cols[:, :, None]
        - free_rows[:, None, :]
    )
    return jnp.sum(counts_real * weight, axis=1)


def per_device(bias, labels, therm_index, counts, free_start, mult_start):
    n_traj = lax.psum(1, "traj")
    n_mstate = lax.psum(1, "mstate")
    states_k = bias.shape[0]
    width = free_start.shape[1]
    col_count = counts.shape[1]
    row_count = counts.shape[2]
    traj_at = lax.axis_index("traj")
    mstate_at = lax.axis_index("mstate")
    col_start = traj_at * col_count
    row_start = mstate_at * row_count
    per_row = row_count // col_count

    col_pairs = []
    for src_t in range(n_traj):
        for c in range(n_mstate):
            dst_t = c * per_row + src_t // n_mstate
            dst_m = src_t % n_mstate
            col_pairs.append((src_t * n_mstate + c, dst_t * n_mstate + dst_m))
    col_offset = (traj_at // n_mstate) * col_count

    states = jax.nn.one_hot(therm_index, states_k, dtype=jnp.float32)
    local_visits = _seg_rows(states, labels, width).T
    bias_t = bias.T
    visits_part = _scatter_blocks(local_visits, "mstate", n_mstate, _add)
    counts_real = counts.astype(jnp.float32)

    free_cols = lax.dynamic_slice_in_dim(free_start, col_start, col_count, 1)
    mult_cols = lax.dynamic_slice_in_dim(mult_start, col_start, col_count, 1)
    free_rows = lax.dynamic_slice_in_dim(free_start, row_start, row_count, 1)
    mult_rows = lax.dynamic_slice_in_dim(mult_start, row_start, row_count, 1)
    visits_rows = None
    for step in range(ITERS):
        partial_rows = _mult_part(counts_real, free_cols, mult_cols, free_rows, mult_rows)
        row_total = _tree(partial_rows, "traj", n_traj, _add)
        if step == 0:
            visits_rows = _tree(visits_part, "traj", n_traj, _add)
        mult_rows = jnp.log(0.5 + row_total)
        level_rows = jnp.log(jnp.exp(mult_rows) + visits_rows) + free_rows
        level = lax.all_gather(level_rows.reshape(-1), "mstate", tiled=True)
        level_t = jnp.transpose(level.reshape(n_mstate, states_k, row_count), (0, 2, 1)).reshape(width, states_k)
        local_top, local_total = _frame_part(level_t, bias_t, labels, width)
        packed = _scatter_blocks(local_total, "mstate", n_mstate, _lse_merge, local_top[:, None])
        packed = _tree(packed, "traj", n_traj, _lse_merge)
        free_rows = -(packed[:, -1:] + jnp.log(packed[:, :-1]))
        if step + 1 < ITERS:
            block = jnp.stack([
                lax.dynamic_slice_in_dim(free_rows, col_offset, col_count, 1),
                lax.dynamic_slice_in_dim(mult_rows, col_offset, col_count, 1),
            ])
            block = _send(block, ("traj", "mstate"), col_pairs)
            free_cols, mult_cols = block[0], block[1]
    return (free_rows, mult_rows)


def solution(mesh):
    placed = (
        P(None, ("traj", "mstate")),
        P(("traj", "mstate")),
        P(("traj", "mstate")),
        P(None, "traj", "mstate"),
        P(),
        P(),
    )
    return jax.shard_map(
        per_device,
        mesh=mesh,
        in_specs=placed,
        out_specs=(P(None, "mstate"), P(None, "mstate")),
        check_vma=False,
    )
```

```python
import jax
import jax.numpy as jnp
from jax import lax
from jax.experimental import pallas as pl
from jax.experimental.pallas import tpu as pltpu
from jax.sharding import PartitionSpec as P

ITERS = 2


def _xor_pairs(n, bit):
    return [(i, i ^ bit) for i in range(n)]


def _send(x, axis, pairs):
    return lax.ppermute(x.reshape(-1), axis, pairs).reshape(x.shape)


def _add(a, b):
    return a + b


def _lse_merge(a, b):
    top = jnp.maximum(a[:, -1:], b[:, -1:])
    body = a[:, :-1] * jnp.exp(a[:, -1:] - top) + b[:, :-1] * jnp.exp(b[:, -1:] - top)
    return jnp.concatenate([body, top], axis=1)


def _tree(x, axis, n, merge):
    shift = 1
    while shift < n:
        wide = 4 if shift * 4 <= n else 2
        got = [_send(x, axis, _xor_pairs(n, j * shift)) for j in range(1, wide)]
        if wide == 4:
            x = merge(merge(x, got[0]), merge(got[1], got[2]))
        else:
            x = merge(x, got[0])
        shift *= wide
    return x


def _scatter_blocks(x, axis, n, merge, extra=None):
    index = lax.axis_index(axis)
    width = x.shape[1] // n

    def block(b):
        piece = lax.dynamic_slice_in_dim(x, b * width, width, 1)
        return piece if extra is None else jnp.concatenate([piece, extra], axis=1)

    own = block(index)
    got = [_send(block(index ^ j), axis, _xor_pairs(n, j)) for j in range(1, n)]
    while got:
        own = merge(own, got.pop(0))
    return own


def _gather_blocks(x, axis, n):
    index = lax.axis_index(axis)
    width = x.shape[1]
    full = jnp.zeros((x.shape[0], width * n), x.dtype)
    full = lax.dynamic_update_slice_in_dim(full, x, index * width, 1)
    for j in range(1, n):
        got = _send(x, axis, _xor_pairs(n, j))
        full = lax.dynamic_update_slice_in_dim(full, got, (index ^ j) * width, 1)
    return full


def _scatter_kernel(lab_ref, w_ref, o_ref, *accs):
    unroll = len(accs)
    for acc in accs:
        acc[...] = jnp.zeros_like(acc)

    def body(c, carry):
        base = c * unroll
        for j in range(unroll):
            x = base + j
            i = lab_ref[x]
            accs[j][pl.ds(i, 1), :] += w_ref[pl.ds(x, 1), :]
        return carry

    lax.fori_loop(0, w_ref.shape[0] // unroll, body, 0)
    total = accs[0][...]
    for acc in accs[1:]:
        total = total + acc[...]
    o_ref[...] = total


def _seg_rows(w_t, labels, width, unroll=16):
    return pl.pallas_call(
        _scatter_kernel,
        in_specs=[pl.BlockSpec(memory_space=pltpu.SMEM), pl.BlockSpec(memory_space=pltpu.VMEM)],
        out_specs=pl.BlockSpec(memory_space=pltpu.VMEM),
        out_shape=jax.ShapeDtypeStruct((width, w_t.shape[1]), jnp.float32),
        scratch_shapes=[pltpu.VMEM((width, w_t.shape[1]), jnp.float32)] * unroll,
    )(labels, w_t)


def _gather_kernel(lab_ref, lev_ref, o_ref):
    unroll = 32

    def body(c, carry):
        base = c * unroll
        for j in range(unroll):
            x = base + j
            o_ref[pl.ds(x, 1), :] = lev_ref[pl.ds(lab_ref[x], 1), :]
        return carry

    lax.fori_loop(0, o_ref.shape[0] // unroll, body, 0)


def _take_rows(lev_t, labels):
    return pl.pallas_call(
        _gather_kernel,
        in_specs=[pl.BlockSpec(memory_space=pltpu.SMEM), pl.BlockSpec(memory_space=pltpu.VMEM)],
        out_specs=pl.BlockSpec(memory_space=pltpu.VMEM),
        out_shape=jax.ShapeDtypeStruct((labels.shape[0], lev_t.shape[1]), lev_t.dtype),
    )(labels, lev_t)


def _frame_part(level, bias_t, labels, width):
    scores = _take_rows(level.T, labels) - bias_t
    top = jnp.max(scores, axis=1)
    logl = top + jnp.log(jnp.sum(jnp.exp(scores - top[:, None]), axis=1))
    term = -bias_t - logl[:, None]
    local_top = jnp.max(term, axis=0)
    weights = jnp.exp(term - local_top[None, :])
    local_total = _seg_rows(weights, labels, width).T
    return local_top, local_total


def _mult_part(counts_real, free_cols, mult_cols, free_rows, mult_rows):
    weight = jax.nn.sigmoid(
        mult_rows[:, None, :]
        + free_cols[:, :, None]
        - mult_cols[:, :, None]
        - free_rows[:, None, :]
    )
    return jnp.sum(counts_real * weight, axis=1)


def per_device(bias, labels, therm_index, counts, free_start, mult_start):
    n_traj = lax.psum(1, "traj")
    n_mstate = lax.psum(1, "mstate")
    states_k = bias.shape[0]
    width = free_start.shape[1]
    col_count = counts.shape[1]
    row_count = counts.shape[2]
    traj_at = lax.axis_index("traj")
    mstate_at = lax.axis_index("mstate")
    col_start = traj_at * col_count
    row_start = mstate_at * row_count
    per_row = row_count // col_count

    col_pairs = []
    for src_t in range(n_traj):
        for c in range(n_mstate):
            dst_t = c * per_row + src_t // n_mstate
            dst_m = src_t % n_mstate
            col_pairs.append((src_t * n_mstate + c, dst_t * n_mstate + dst_m))
    col_offset = (traj_at // n_mstate) * col_count

    states = jax.nn.one_hot(therm_index, states_k, dtype=jnp.float32)
    local_visits = _seg_rows(states, labels, width).T
    bias_t = bias.T
    visits_part = _scatter_blocks(local_visits, "mstate", n_mstate, _add)
    counts_real = counts.astype(jnp.float32)

    free_cols = lax.dynamic_slice_in_dim(free_start, col_start, col_count, 1)
    mult_cols = lax.dynamic_slice_in_dim(mult_start, col_start, col_count, 1)
    free_rows = lax.dynamic_slice_in_dim(free_start, row_start, row_count, 1)
    mult_rows = lax.dynamic_slice_in_dim(mult_start, row_start, row_count, 1)
    visits_rows = None
    for step in range(ITERS):
        partial_rows = _mult_part(counts_real, free_cols, mult_cols, free_rows, mult_rows)
        row_total = _tree(partial_rows, "traj", n_traj, _add)
        if step == 0:
            visits_rows = _tree(visits_part, "traj", n_traj, _add)
        mult_rows = jnp.log(0.5 + row_total)
        level_rows = jnp.log(jnp.exp(mult_rows) + visits_rows) + free_rows
        level = _gather_blocks(level_rows, "mstate", n_mstate)
        local_top, local_total = _frame_part(level, bias_t, labels, width)
        packed = _scatter_blocks(local_total, "mstate", n_mstate, _lse_merge, local_top[:, None])
        packed = _tree(packed, "traj", n_traj, _lse_merge)
        free_rows = -(packed[:, -1:] + jnp.log(packed[:, :-1]))
        if step + 1 < ITERS:
            block = jnp.stack([
                lax.dynamic_slice_in_dim(free_rows, col_offset, col_count, 1),
                lax.dynamic_slice_in_dim(mult_rows, col_offset, col_count, 1),
            ])
            block = _send(block, ("traj", "mstate"), col_pairs)
            free_cols, mult_cols = block[0], block[1]
    return (free_rows, mult_rows)


def solution(mesh):
    placed = (
        P(None, ("traj", "mstate")),
        P(("traj", "mstate")),
        P(("traj", "mstate")),
        P(None, "traj", "mstate"),
        P(),
        P(),
    )
    return jax.shard_map(
        per_device,
        mesh=mesh,
        in_specs=placed,
        out_specs=(P(None, "mstate"), P(None, "mstate")),
        check_vma=False,
    )
```
